128 devices in a mesh: dp: 16 (over y, z), cent: 8 (over x, core).
Axes of the slice: x: 4, y: 4, z: 4, core: 2. Of those that a mesh axis runs over, the one named last changes fastest.
Arguments:
- embeddings: bfloat16 [12288, 768], P('dp'), may hold values from -40 to 40
- centroids: bfloat16 [32768, 768], P('cent'), may hold values from -5 to 5
- rotation: float32 [768, 768], replicated, may hold values from -1 to 2
Outputs:
- new_centroids: float32 [32768, 768], P(('cent', 'dp'))
- new_rotation: float32 [768, 768], replicated
The draws below stay inside these ranges and needn't reach their ends.
All inputs are finite; a program needn't handle non-finite values.
Results may differ from the reference program's by a relative error of at most 0.0042.
Values sent between devices are 32-bit elements; how exact they have to be, the bound alone decides.
No kernel may reach another device: no remote copies, remote signals or barrier semaphores. Data moves between devices by JAX's collectives and lax.ppermute only.
A program may use at most 128 MiB of HBM per device.

```python
import math
import jax
import jax.numpy as jnp
from jax import lax

D = 768
ROWS_DEV = 768
NS_ITERS = 4
CENTROIDS = 32768
ROWS = 12288


def base_rows(key):
    return jnp.clip(jax.random.normal(jax.random.fold_in(key, 99), (CENTROIDS, D), jnp.float32), -5.0, 5.0)


def draw_embeddings(key, part):
    values = jnp.clip(jax.random.normal(jax.random.fold_in(key, 1), (ROWS, D), jnp.float32), -6.0, 6.0)
    return values.astype(jnp.bfloat16)


def draw_centroids(key, part):
    values = base_rows(key)
    return values.astype(jnp.bfloat16)


def draw_rotation(key, part):
    noise = jnp.clip(jax.random.normal(jax.random.fold_in(key, 4), (D, D), jnp.float32), -4.0, 4.0)
    return (jnp.eye(D, dtype=jnp.float32) + 0.5 / math.sqrt(D) * noise).astype(jnp.float32)


def setup_inputs(seed: int = 0) -> dict:
    splits = jax.random.split(jax.random.key(seed), 4)
    return {
        "embeddings": draw_embeddings(jax.random.fold_in(splits[3], 71), 0),
        "centroids": draw_centroids(jax.random.fold_in(splits[3], 71), 0),
        "rotation": draw_rotation(jax.random.fold_in(splits[3], 71), 0),
    }


SHARPNESS = 3.0
PRIOR_WEIGHT = 0.25
EPSILON = 1e-06

def polar_update(cross_gram):
    highest = lax.Precision.HIGHEST
    frobenius = jnp.sqrt(jnp.sum(cross_gram * cross_gram) + EPSILON)
    unit_cross = cross_gram / frobenius
    gram_once = jnp.dot(unit_cross.T, unit_cross, precision=highest)
    gram_twice = jnp.dot(gram_once, gram_once, precision=highest)
    norm_scale = (jnp.sum(gram_twice * gram_twice) + EPSILON) ** 0.125
    iterate = unit_cross / norm_scale
    for iteration in range(NS_ITERS):
        inner = jnp.dot(iterate.T, iterate, precision=highest)
        iterate = 1.5 * iterate - 0.5 * jnp.dot(iterate, inner, precision=highest)
    return iterate

def reference(embeddings, centroids, rotation):
    highest = lax.Precision.HIGHEST
    half_norm = 0.5 * lax.optimization_barrier(jnp.sum(jnp.square(centroids.astype(jnp.float32)), axis=1))
    score_scale = SHARPNESS / math.sqrt(D)
    block_count = ROWS // ROWS_DEV
    emb_blocks = embeddings.reshape(block_count, ROWS_DEV, D)

    def one_block(carry, row_block):
        cent_sums, counts, cross_gram = carry
        rows_wide = row_block.astype(jnp.float32)
        rotated = jnp.dot(rows_wide, rotation, precision=highest).astype(jnp.bfloat16)
        scores = (jnp.dot(rotated, centroids.T, preferred_element_type=jnp.float32) - half_norm[None, :]) * score_scale
        row_top = lax.optimization_barrier(jnp.max(scores, axis=1))
        exp_scores = jnp.exp(scores - row_top[:, None])
        row_total = lax.optimization_barrier(jnp.sum(exp_scores, axis=1))
        weights = (exp_scores / row_total[:, None]).astype(jnp.bfloat16)
        cent_sums = cent_sums + jnp.dot(weights.T, rotated, preferred_element_type=jnp.float32)
        counts = counts + lax.optimization_barrier(jnp.sum(weights.astype(jnp.float32), axis=0))
        rebuilt = jnp.dot(weights, centroids, preferred_element_type=jnp.float32)
        cross_gram = cross_gram + jnp.dot(rows_wide.T, rebuilt, precision=highest)
        return ((cent_sums, counts, cross_gram), None)
    start_state = (jnp.zeros((CENTROIDS, D), jnp.float32), jnp.zeros((CENTROIDS,), jnp.float32), jnp.zeros((D, D), jnp.float32))
    (cent_sums, counts, cross_gram), unused = lax.scan(one_block, start_state, emb_blocks)
    new_centroids = (cent_sums + PRIOR_WEIGHT * centroids.astype(jnp.float32)) / (counts + PRIOR_WEIGHT)[:, None]
    return (new_centroids, polar_update(cross_gram))
```

```python
import math

import jax
import jax.numpy as jnp
from jax import lax
from jax.sharding import PartitionSpec as P

NS_ITERS = 4

STEPS = (("cent", 0), ("cent", 1), ("dp", 0), ("dp", 2), ("cent", 2), ("dp", 1), ("dp", 3))


def _pairs(axis, bit):
    size = lax.axis_size(axis)
    return [(i, i ^ (1 << bit)) for i in range(size)]


def ring_psum(x, steps=STEPS):
    buf = x
    for axis, bit in steps:
        half = buf.shape[0] // 2
        low, high = buf[:half], buf[half:]
        upper = ((lax.axis_index(axis) >> bit) & 1) == 1
        send = jnp.where(upper, low, high)
        keep = jnp.where(upper, high, low)
        buf = keep + lax.ppermute(send, axis, _pairs(axis, bit))
    for axis, bit in reversed(steps):
        upper = ((lax.axis_index(axis) >> bit) & 1) == 1
        other = lax.ppermute(buf, axis, _pairs(axis, bit))
        buf = jnp.where(upper, jnp.concatenate([other, buf]), jnp.concatenate([buf, other]))
    return buf


SHARPNESS = 3.0
PRIOR_WEIGHT = 0.25
EPSILON = 1e-06


def split3(x):
    first = lax.reduce_precision(x, exponent_bits=8, mantissa_bits=7)
    rest = x - first
    second = lax.reduce_precision(rest, exponent_bits=8, mantissa_bits=7)
    third = rest - second
    return first.astype(jnp.bfloat16), second.astype(jnp.bfloat16), third.astype(jnp.bfloat16)


def body(embeddings, centroids, rotation):
    high = lax.Precision.HIGH
    width = rotation.shape[0]
    dp_idx = lax.axis_index("dp")

    rot_pieces = jnp.concatenate(split3(rotation), axis=0)
    emb_stacked = jnp.concatenate([embeddings] * 3, axis=1)
    rotated = jnp.dot(emb_stacked, rot_pieces, preferred_element_type=jnp.float32).astype(jnp.bfloat16)

    half_norm = 0.5 * jnp.sum(jnp.square(centroids.astype(jnp.float32)), axis=1)
    score_scale = SHARPNESS / math.sqrt(width)
    raw_scores = lax.dot_general(
        rotated, centroids, (((1,), (1,)), ((), ())), preferred_element_type=jnp.float32
    )
    scores = (raw_scores - half_norm[None, :]) * score_scale
    local_top = jnp.max(scores, axis=1)
    local_total = jnp.sum(jnp.exp(scores - local_top[:, None]), axis=1)
    stats = lax.all_gather(jnp.stack([local_top, local_total]), "cent")
    row_top = jnp.max(stats[:, 0, :], axis=0)
    row_total = jnp.sum(stats[:, 1, :] * jnp.exp(stats[:, 0, :] - row_top[None, :]), axis=0)
    exp_scores = jnp.exp(scores - row_top[:, None])
    weights = (exp_scores / row_total[:, None]).astype(jnp.bfloat16)

    rebuilt = jnp.dot(weights, centroids, preferred_element_type=jnp.float32)
    reb_pieces = jnp.concatenate(split3(rebuilt), axis=0)
    emb_rows = jnp.concatenate([embeddings] * 3, axis=0)
    partial_value = lax.dot_general(
        emb_rows, reb_pieces, (((0,), (0,)), ((), ())), preferred_element_type=jnp.float32
    )

    cross_gram = ring_psum(partial_value)

    ones = jnp.zeros((rotated.shape[0], 128), jnp.bfloat16).at[:, 0].set(1)
    rotated_ones = jnp.concatenate([rotated, ones], axis=1)
    cent_sums = lax.dot_general(
        weights, rotated_ones, (((0,), (0,)), ((), ())), preferred_element_type=jnp.float32
    )
    share = lax.psum_scatter(cent_sums, "dp", scatter_dimension=0, tiled=True)
    share_sums = share[:, :width]
    share_counts = share[:, width]
    block_rows = share.shape[0]
    first_row = dp_idx * block_rows
    own_centroids = lax.dynamic_slice_in_dim(centroids, first_row, block_rows, 0).astype(
        jnp.float32
    )
    new_centroids = (share_sums + PRIOR_WEIGHT * own_centroids) / (share_counts + PRIOR_WEIGHT)[
        :, None
    ]

    frobenius = jnp.sqrt(jnp.sum(cross_gram * cross_gram) + EPSILON)
    unit_cross = cross_gram / frobenius
    gram_once = jnp.dot(unit_cross.T, unit_cross, precision=high)
    gram_twice = jnp.dot(gram_once, gram_once, precision=high)
    norm_scale = (jnp.sum(gram_twice * gram_twice) + EPSILON) ** 0.125
    iterate = unit_cross / norm_scale
    for iteration in range(NS_ITERS):
        inner = jnp.dot(iterate.T, iterate, precision=high)
        iterate = 1.5 * iterate - 0.5 * jnp.dot(iterate, inner, precision=high)
    return (new_centroids, iterate)


def solution(mesh):
    in_specs = (P("dp", None), P("cent", None), P())
    out_specs = (P(("cent", "dp"), None), P())
    return jax.shard_map(body, mesh=mesh, in_specs=in_specs, out_specs=out_specs, check_vma=False)
```

```python
import math

import jax
import jax.numpy as jnp
from jax import lax
from jax.sharding import PartitionSpec as P


NS_ITERS = 4

STEPS = (("cent", 0), ("cent", 1), ("cent", 2), ("dp", 0), ("dp", 2), ("dp", 1), ("dp", 3))


def _pairs(axis, bit):
    size = lax.axis_size(axis)
    return [(i, i ^ (1 << bit)) for i in range(size)]


def ring_psum(x, steps=STEPS):
    buf = x
    for axis, bit in steps:
        half = buf.shape[0] // 2
        low, high = buf[:half], buf[half:]
        upper = ((lax.axis_index(axis) >> bit) & 1) == 1
        send = jnp.where(upper, low, high)
        keep = jnp.where(upper, high, low)
        buf = keep + lax.ppermute(send, axis, _pairs(axis, bit))
    for axis, bit in reversed(steps):
        upper = ((lax.axis_index(axis) >> bit) & 1) == 1
        other = lax.ppermute(buf, axis, _pairs(axis, bit))
        buf = jnp.where(upper, jnp.concatenate([other, buf]), jnp.concatenate([buf, other]))
    return buf


SHARPNESS = 3.0
PRIOR_WEIGHT = 0.25
EPSILON = 1e-06


def split3(x):
    first = lax.reduce_precision(x, exponent_bits=8, mantissa_bits=7)
    rest = x - first
    second = lax.reduce_precision(rest, exponent_bits=8, mantissa_bits=7)
    third = rest - second
    return first.astype(jnp.bfloat16), second.astype(jnp.bfloat16), third.astype(jnp.bfloat16)


def step_body(embeddings, centroids, rotation):
    high = lax.Precision.HIGH
    width = rotation.shape[0]
    dp_idx = lax.axis_index("dp")

    rot_pieces = jnp.concatenate(split3(rotation), axis=0)
    emb_stacked = jnp.concatenate([embeddings] * 3, axis=1)
    rotated = jnp.dot(emb_stacked, rot_pieces, preferred_element_type=jnp.float32).astype(jnp.bfloat16)

    half_norm = 0.5 * jnp.sum(jnp.square(centroids.astype(jnp.float32)), axis=1)
    score_scale = SHARPNESS / math.sqrt(width)
    raw_scores = lax.dot_general(
        rotated, centroids, (((1,), (1,)), ((), ())), preferred_element_type=jnp.float32
    )
    scores = (raw_scores - half_norm[None, :]) * score_scale
    local_top = jnp.max(scores, axis=1)
    local_total = jnp.sum(jnp.exp(scores - local_top[:, None]), axis=1)
    stats = lax.all_gather(jnp.stack([local_top, local_total]), "cent")
    row_top = jnp.max(stats[:, 0, :], axis=0)
    row_total = jnp.sum(stats[:, 1, :] * jnp.exp(stats[:, 0, :] - row_top[None, :]), axis=0)
    exp_scores = jnp.exp(scores - row_top[:, None])
    weights = (exp_scores / row_total[:, None]).astype(jnp.bfloat16)

    rebuilt = jnp.dot(weights, centroids, preferred_element_type=jnp.float32)
    reb_pieces = jnp.concatenate(split3(rebuilt), axis=0)
    emb_rows = jnp.concatenate([embeddings] * 3, axis=0)
    partial_value = lax.dot_general(
        emb_rows, reb_pieces, (((0,), (0,)), ((), ())), preferred_element_type=jnp.float32
    )

    cross_gram = ring_psum(partial_value)

    ones = jnp.zeros((rotated.shape[0], 128), jnp.bfloat16).at[:, 0].set(1)
    rotated_ones = jnp.concatenate([rotated, ones], axis=1)
    cent_sums = lax.dot_general(
        weights, rotated_ones, (((0,), (0,)), ((), ())), preferred_element_type=jnp.float32
    )
    share = lax.psum_scatter(cent_sums, "dp", scatter_dimension=0, tiled=True)
    share_sums = share[:, :width]
    share_counts = share[:, width]
    block_rows = share.shape[0]
    first_row = dp_idx * block_rows
    own_centroids = lax.dynamic_slice_in_dim(centroids, first_row, block_rows, 0).astype(
        jnp.float32
    )
    new_centroids = (share_sums + PRIOR_WEIGHT * own_centroids) / (share_counts + PRIOR_WEIGHT)[
        :, None
    ]

    frobenius = jnp.sqrt(jnp.sum(cross_gram * cross_gram) + EPSILON)
    unit_cross = cross_gram / frobenius
    gram_once = jnp.dot(unit_cross.T, unit_cross, precision=high)
    gram_twice = jnp.dot(gram_once, gram_once, precision=high)
    norm_scale = (jnp.sum(gram_twice * gram_twice) + EPSILON) ** 0.125
    iterate = unit_cross / norm_scale
    for _ in range(NS_ITERS):
        inner = jnp.dot(iterate.T, iterate, precision=high)
        iterate = 1.5 * iterate - 0.5 * jnp.dot(iterate, inner, precision=high)
    return (new_centroids, iterate)


def solution(mesh):
    in_specs = (P("dp", None), P("cent", None), P())
    out_specs = (P(("cent", "dp"), None), P())
    return jax.shard_map(step_body, mesh=mesh, in_specs=in_specs, out_specs=out_specs, check_vma=False)
```

```python
import math

import jax
import jax.numpy as jnp
from jax import lax
from jax.sharding import PartitionSpec as P


NS_ITERS = 4

GROUPS = (("cent", 0, 2), ("cent", 1, 4), ("dp", 0, 4), ("dp", 2, 4))


def _position(axis, bit, radix):
    return (lax.axis_index(axis) >> bit) % radix


def _shift_pairs(axis, bit, radix, shift):
    size = lax.axis_size(axis)
    pairs = []
    for i in range(size):
        p = (i >> bit) % radix
        q = (p + shift) % radix
        pairs.append((i, i + ((q - p) << bit)))
    return pairs


def ring_psum(x, groups=GROUPS):
    buf = x
    for axis, bit, radix in groups:
        part = buf.shape[0] // radix
        p = _position(axis, bit, radix)
        total = lax.dynamic_slice_in_dim(buf, p * part, part, 0)
        for shift in range(1, radix):
            piece = lax.dynamic_slice_in_dim(buf, ((p + shift) % radix) * part, part, 0)
            total = total + lax.ppermute(piece, axis, _shift_pairs(axis, bit, radix, shift))
        buf = total
    for axis, bit, radix in reversed(groups):
        p = _position(axis, bit, radix)
        got = [buf] + [lax.ppermute(buf, axis, _shift_pairs(axis, bit, radix, s)) for s in range(1, radix)]
        ordered = jnp.stack([got[(-j) % radix] for j in range(radix)])
        ordered = jnp.concatenate([ordered, ordered])
        blocks = lax.dynamic_slice_in_dim(ordered, (radix - p) % radix, radix, 0)
        buf = blocks.reshape((-1,) + buf.shape[1:])
    return buf


SHARPNESS = 3.0
PRIOR_WEIGHT = 0.25
EPSILON = 1e-06


def split3(x):
    first = lax.reduce_precision(x, exponent_bits=8, mantissa_bits=7)
    rest = x - first
    second = lax.reduce_precision(rest, exponent_bits=8, mantissa_bits=7)
    third = rest - second
    return first.astype(jnp.bfloat16), second.astype(jnp.bfloat16), third.astype(jnp.bfloat16)


def step_body(embeddings, centroids, rotation):
    high = lax.Precision.HIGH
    width = rotation.shape[0]
    dp_idx = lax.axis_index("dp")

    rot_pieces = jnp.concatenate(split3(rotation), axis=0)
    emb_stacked = jnp.concatenate([embeddings] * 3, axis=1)
    rotated = jnp.dot(emb_stacked, rot_pieces, preferred_element_type=jnp.float32).astype(jnp.bfloat16)

    half_norm = 0.5 * jnp.sum(jnp.square(centroids.astype(jnp.float32)), axis=1)
    score_scale = SHARPNESS / math.sqrt(width)
    raw_scores = lax.dot_general(
        rotated, centroids, (((1,), (1,)), ((), ())), preferred_element_type=jnp.float32
    )
    scores = (raw_scores - half_norm[None, :]) * score_scale
    local_top = jnp.max(scores, axis=1)
    local_total = jnp.sum(jnp.exp(scores - local_top[:, None]), axis=1)
    stats = lax.all_gather(jnp.stack([local_top, local_total]), "cent")
    row_top = jnp.max(stats[:, 0, :], axis=0)
    row_total = jnp.sum(stats[:, 1, :] * jnp.exp(stats[:, 0, :] - row_top[None, :]), axis=0)
    exp_scores = jnp.exp(scores - row_top[:, None])
    weights = (exp_scores / row_total[:, None]).astype(jnp.bfloat16)

    rebuilt = jnp.dot(weights, centroids, preferred_element_type=jnp.float32)
    reb_pieces = jnp.concatenate(split3(rebuilt), axis=0)
    emb_rows = jnp.concatenate([embeddings] * 3, axis=0)
    partial_value = lax.dot_general(
        emb_rows, reb_pieces, (((0,), (0,)), ((), ())), preferred_element_type=jnp.float32
    )

    cross_gram = ring_psum(partial_value)

    ones = jnp.zeros((rotated.shape[0], 128), jnp.bfloat16).at[:, 0].set(1)
    rotated_ones = jnp.concatenate([rotated, ones], axis=1)
    cent_sums = lax.dot_general(
        weights, rotated_ones, (((0,), (0,)), ((), ())), preferred_element_type=jnp.float32
    )
    share = lax.psum_scatter(cent_sums, "dp", scatter_dimension=0, tiled=True)
    share_sums = share[:, :width]
    share_counts = share[:, width]
    block_rows = share.shape[0]
    first_row = dp_idx * block_rows
    own_centroids = lax.dynamic_slice_in_dim(centroids, first_row, block_rows, 0).astype(
        jnp.float32
    )
    new_centroids = (share_sums + PRIOR_WEIGHT * own_centroids) / (share_counts + PRIOR_WEIGHT)[
        :, None
    ]

    frobenius = jnp.sqrt(jnp.sum(cross_gram * cross_gram) + EPSILON)
    unit_cross = cross_gram / frobenius
    gram_once = jnp.dot(unit_cross.T, unit_cross, precision=high)
    gram_twice = jnp.dot(gram_once, gram_once, precision=high)
    norm_scale = (jnp.sum(gram_twice * gram_twice) + EPSILON) ** 0.125
    iterate = unit_cross / norm_scale
    for _ in range(NS_ITERS):
        inner = jnp.dot(iterate.T, iterate, precision=high)
        iterate = 1.5 * iterate - 0.5 * jnp.dot(iterate, inner, precision=high)
    return (new_centroids, iterate)


def solution(mesh):
    in_specs = (P("dp", None), P("cent", None), P())
    out_specs = (P(("cent", "dp"), None), P())
    return jax.shard_map(step_body, mesh=mesh, in_specs=in_specs, out_specs=out_specs, check_vma=False)
```

```python
import math

import jax
import jax.numpy as jnp
from jax import lax
from jax.sharding import PartitionSpec as P


NS_ITERS = 4

GROUPS = (("cent", 0, 2), ("cent", 1, 4), ("dp", 0, 4), ("dp", 2, 4))


def _position(axis, bit, radix):
    return (lax.axis_index(axis) >> bit) % radix


def _shift_pairs(axis, bit, radix, shift):
    size = lax.axis_size(axis)
    pairs = []
    for i in range(size):
        p = (i >> bit) % radix
        q = (p + shift) % radix
        pairs.append((i, i + ((q - p) << bit)))
    return pairs


def ring_psum(x, groups=GROUPS):
    buf = x
    for axis, bit, radix in groups:
        part = buf.shape[0] // radix
        p = _position(axis, bit, radix)
        total = lax.dynamic_slice_in_dim(buf, p * part, part, 0)
        for shift in range(1, radix):
            piece = lax.dynamic_slice_in_dim(buf, ((p + shift) % radix) * part, part, 0)
            total = total + lax.ppermute(piece, axis, _shift_pairs(axis, bit, radix, shift))
        buf = total
    for axis, bit, radix in reversed(groups):
        p = _position(axis, bit, radix)
        got = [buf] + [lax.ppermute(buf, axis, _shift_pairs(axis, bit, radix, s)) for s in range(1, radix)]
        ordered = jnp.stack([got[(-j) % radix] for j in range(radix)])
        ordered = jnp.concatenate([ordered, ordered])
        blocks = lax.dynamic_slice_in_dim(ordered, (radix - p) % radix, radix, 0)
        buf = blocks.reshape((-1,) + buf.shape[1:])
    return buf


SHARPNESS = 3.0
PRIOR_WEIGHT = 0.25
EPSILON = 1e-06


def split3(x):
    first = lax.reduce_precision(x, exponent_bits=8, mantissa_bits=7)
    rest = x - first
    second = lax.reduce_precision(rest, exponent_bits=8, mantissa_bits=7)
    third = rest - second
    return first.astype(jnp.bfloat16), second.astype(jnp.bfloat16), third.astype(jnp.bfloat16)


def step_body(embeddings, centroids, rotation):
    high = lax.Precision.HIGH
    width = rotation.shape[0]
    dp_idx = lax.axis_index("dp")

    rot_pieces = jnp.concatenate(split3(rotation), axis=0)
    emb_stacked = jnp.concatenate([embeddings] * 3, axis=1)
    rotated = jnp.dot(emb_stacked, rot_pieces, preferred_element_type=jnp.float32).astype(jnp.bfloat16)

    half_norm = 0.5 * jnp.sum(jnp.square(centroids.astype(jnp.float32)), axis=1)
    score_scale = SHARPNESS / math.sqrt(width)
    raw_scores = lax.dot_general(
        rotated, centroids, (((1,), (1,)), ((), ())), preferred_element_type=jnp.float32
    )
    scores = (raw_scores - half_norm[None, :]) * score_scale
    local_top = jnp.max(scores, axis=1)
    local_total = jnp.sum(jnp.exp(scores - local_top[:, None]), axis=1)
    stats = lax.all_gather(jnp.stack([local_top, local_total]), "cent")
    row_top = jnp.max(stats[:, 0, :], axis=0)
    row_total = jnp.sum(stats[:, 1, :] * jnp.exp(stats[:, 0, :] - row_top[None, :]), axis=0)
    exp_scores = jnp.exp(scores - row_top[:, None])
    weights = (exp_scores / row_total[:, None]).astype(jnp.bfloat16)

    rebuilt = jnp.dot(weights, centroids, preferred_element_type=jnp.float32)
    reb_high = lax.reduce_precision(rebuilt, exponent_bits=8, mantissa_bits=7)
    reb_pieces = jnp.concatenate(
        [reb_high.astype(jnp.bfloat16), (rebuilt - reb_high).astype(jnp.bfloat16)], axis=0
    )
    emb_rows = jnp.concatenate([embeddings] * 2, axis=0)
    partial_value = lax.dot_general(
        emb_rows, reb_pieces, (((0,), (0,)), ((), ())), preferred_element_type=jnp.float32
    )

    counts = jnp.sum(weights.astype(jnp.float32), axis=0)
    n_cent = centroids.shape[0]
    cent_idx = lax.axis_index("cent")
    radix = math.prod(group[2] for group in GROUPS)
    need_rows = -(-lax.axis_size("cent") * n_cent // width)
    slot_rows = -(-(width + need_rows) // radix) * radix - width
    slots = jnp.zeros((slot_rows * width,), jnp.float32)
    slots = lax.dynamic_update_slice_in_dim(slots, counts, cent_idx * n_cent, 0)
    packed = ring_psum(jnp.concatenate([partial_value, slots.reshape(slot_rows, width)], axis=0))
    cross_gram = packed[:width]
    all_counts = packed[width:].reshape(-1)

    cent_sums = lax.dot_general(
        weights, rotated, (((0,), (0,)), ((), ())), preferred_element_type=jnp.float32
    )
    share_sums = lax.psum_scatter(cent_sums, "dp", scatter_dimension=0, tiled=True)
    block_rows = share_sums.shape[0]
    first_row = dp_idx * block_rows
    share_counts = lax.dynamic_slice_in_dim(all_counts, cent_idx * n_cent + first_row, block_rows, 0)
    own_centroids = lax.dynamic_slice_in_dim(centroids, first_row, block_rows, 0).astype(
        jnp.float32
    )
    new_centroids = (share_sums + PRIOR_WEIGHT * own_centroids) / (share_counts + PRIOR_WEIGHT)[
        :, None
    ]

    frobenius = jnp.sqrt(jnp.sum(cross_gram * cross_gram) + EPSILON)
    unit_cross = cross_gram / frobenius
    gram_once = jnp.dot(unit_cross.T, unit_cross, precision=high)
    gram_twice = jnp.dot(gram_once, gram_once, precision=high)
    norm_scale = (jnp.sum(gram_twice * gram_twice) + EPSILON) ** 0.125
    iterate = unit_cross / norm_scale
    for iteration in range(NS_ITERS):
        if iteration == 0:
            inner = gram_once / (norm_scale * norm_scale)
        else:
            inner = jnp.dot(iterate.T, iterate, precision=high)
        iterate = 1.5 * iterate - 0.5 * jnp.dot(iterate, inner, precision=high)
    return (new_centroids, iterate)


def solution(mesh):
    in_specs = (P("dp", None), P("cent", None), P())
    out_specs = (P(("cent", "dp"), None), P())
    return jax.shard_map(step_body, mesh=mesh, in_specs=in_specs, out_specs=out_specs, check_vma=False)
```

```python
import math

import jax
import jax.numpy as jnp
from jax import lax
from jax.sharding import PartitionSpec as P


NS_ITERS = 4

GROUPS = (("cent", 0, 2), ("cent", 1, 4), ("dp", 0, 4), ("dp", 2, 4))


def _position(axis, bit, radix):
    return (lax.axis_index(axis) >> bit) % radix


def _shift_pairs(axis, bit, radix, shift):
    size = lax.axis_size(axis)
    pairs = []
    for i in range(size):
        p = (i >> bit) % radix
        q = (p + shift) % radix
        pairs.append((i, i + ((q - p) << bit)))
    return pairs


def ring_psum(x, groups=GROUPS):
    buf = x
    for axis, bit, radix in groups:
        part = buf.shape[0] // radix
        p = _position(axis, bit, radix)
        total = lax.dynamic_slice_in_dim(buf, p * part, part, 0)
        for shift in range(1, radix):
            piece = lax.dynamic_slice_in_dim(buf, ((p + shift) % radix) * part, part, 0)
            total = total + lax.ppermute(piece, axis, _shift_pairs(axis, bit, radix, shift))
        buf = total
    for axis, bit, radix in reversed(groups):
        p = _position(axis, bit, radix)
        got = [buf] + [lax.ppermute(buf, axis, _shift_pairs(axis, bit, radix, s)) for s in range(1, radix)]
        ordered = jnp.stack([got[(-j) % radix] for j in range(radix)])
        ordered = jnp.concatenate([ordered, ordered])
        blocks = lax.dynamic_slice_in_dim(ordered, (radix - p) % radix, radix, 0)
        buf = blocks.reshape((-1,) + buf.shape[1:])
    return buf


SHARPNESS = 3.0
PRIOR_WEIGHT = 0.25
EPSILON = 1e-06


def split3(x):
    first = lax.reduce_precision(x, exponent_bits=8, mantissa_bits=7)
    rest = x - first
    second = lax.reduce_precision(rest, exponent_bits=8, mantissa_bits=7)
    third = rest - second
    return first.astype(jnp.bfloat16), second.astype(jnp.bfloat16), third.astype(jnp.bfloat16)


def step_body(embeddings, centroids, rotation):
    high = lax.Precision.HIGH
    width = rotation.shape[0]
    dp_idx = lax.axis_index("dp")

    rot_pieces = jnp.concatenate(split3(rotation), axis=0)
    emb_stacked = jnp.concatenate([embeddings] * 3, axis=1)
    rotated = jnp.dot(emb_stacked, rot_pieces, preferred_element_type=jnp.float32).astype(jnp.bfloat16)

    half_norm = 0.5 * jnp.sum(jnp.square(centroids.astype(jnp.float32)), axis=1)
    score_scale = SHARPNESS / math.sqrt(width)
    raw_scores = lax.dot_general(
        rotated, centroids, (((1,), (1,)), ((), ())), preferred_element_type=jnp.float32
    )
    scores = (raw_scores - half_norm[None, :]) * score_scale
    local_top = jnp.max(scores, axis=1)
    local_total = jnp.sum(jnp.exp(scores - local_top[:, None]), axis=1)
    stats = lax.all_gather(jnp.stack([local_top, local_total]), "cent")
    row_top = jnp.max(stats[:, 0, :], axis=0)
    row_total = jnp.sum(stats[:, 1, :] * jnp.exp(stats[:, 0, :] - row_top[None, :]), axis=0)
    exp_scores = jnp.exp(scores - row_top[:, None])
    weights = (exp_scores / row_total[:, None]).astype(jnp.bfloat16)

    rebuilt = jnp.dot(weights, centroids, preferred_element_type=jnp.float32)
    reb_high = lax.reduce_precision(rebuilt, exponent_bits=8, mantissa_bits=7)
    reb_pieces = jnp.concatenate(
        [reb_high.astype(jnp.bfloat16), (rebuilt - reb_high).astype(jnp.bfloat16)], axis=0
    )
    emb_rows = jnp.concatenate([embeddings] * 2, axis=0)
    partial_value = lax.dot_general(
        emb_rows, reb_pieces, (((0,), (0,)), ((), ())), preferred_element_type=jnp.float32
    )

    cross_gram = ring_psum(partial_value)

    ones = jnp.zeros((rotated.shape[0], 128), jnp.bfloat16).at[:, 0].set(1)
    rotated_ones = jnp.concatenate([rotated, ones], axis=1)
    cent_sums = lax.dot_general(
        weights, rotated_ones, (((0,), (0,)), ((), ())), preferred_element_type=jnp.float32
    )
    share = lax.psum_scatter(cent_sums, "dp", scatter_dimension=0, tiled=True)
    share_sums = share[:, :width]
    share_counts = share[:, width]
    block_rows = share.shape[0]
    first_row = dp_idx * block_rows
    own_centroids = lax.dynamic_slice_in_dim(centroids, first_row, block_rows, 0).astype(
        jnp.float32
    )
    new_centroids = (share_sums + PRIOR_WEIGHT * own_centroids) / (share_counts + PRIOR_WEIGHT)[
        :, None
    ]

    frobenius = jnp.sqrt(jnp.sum(cross_gram * cross_gram) + EPSILON)
    unit_cross = cross_gram / frobenius
    gram_once = jnp.dot(unit_cross.T, unit_cross, precision=high)
    gram_twice = jnp.dot(gram_once, gram_once, precision=high)
    norm_scale = (jnp.sum(gram_twice * gram_twice) + EPSILON) ** 0.125
    iterate = unit_cross / norm_scale
    for iteration in range(NS_ITERS):
        if iteration == 0:
            inner = gram_once / (norm_scale * norm_scale)
        else:
            inner = jnp.dot(iterate.T, iterate, precision=high)
        iterate = 1.5 * iterate - 0.5 * jnp.dot(iterate, inner, precision=high)
    return (new_centroids, iterate)


def solution(mesh):
    in_specs = (P("dp", None), P("cent", None), P())
    out_specs = (P(("cent", "dp"), None), P())
    return jax.shard_map(step_body, mesh=mesh, in_specs=in_specs, out_specs=out_specs, check_vma=False)
```

```python
import math

import jax
import jax.numpy as jnp
from jax import lax
from jax.sharding import PartitionSpec as P


NS_ITERS = 4

GROUPS = (("cent", 0, 2), ("cent", 1, 4), ("dp", 0, 4), ("dp", 2, 4))


CENT_GROUPS = tuple(group for group in GROUPS if group[0] == "cent")


def _position(axis, bit, radix):
    return (lax.axis_index(axis) >> bit) % radix


def _shift_pairs(axis, bit, radix, shift):
    size = lax.axis_size(axis)
    pairs = []
    for i in range(size):
        p = (i >> bit) % radix
        q = (p + shift) % radix
        pairs.append((i, i + ((q - p) << bit)))
    return pairs


def ring_psum(x, groups=GROUPS):
    buf = x
    for axis, bit, radix in groups:
        part = buf.shape[0] // radix
        p = _position(axis, bit, radix)
        total = lax.dynamic_slice_in_dim(buf, p * part, part, 0)
        for shift in range(1, radix):
            piece = lax.dynamic_slice_in_dim(buf, ((p + shift) % radix) * part, part, 0)
            total = total + lax.ppermute(piece, axis, _shift_pairs(axis, bit, radix, shift))
        buf = total
    return ring_gather(buf, groups)


def ring_gather(buf, groups=GROUPS):
    for axis, bit, radix in reversed(groups):
        p = _position(axis, bit, radix)
        got = [buf] + [lax.ppermute(buf, axis, _shift_pairs(axis, bit, radix, s)) for s in range(1, radix)]
        ordered = jnp.stack([got[(-j) % radix] for j in range(radix)])
        ordered = jnp.concatenate([ordered, ordered])
        blocks = lax.dynamic_slice_in_dim(ordered, (radix - p) % radix, radix, 0)
        buf = blocks.reshape((-1,) + buf.shape[1:])
    return buf


SHARPNESS = 3.0
PRIOR_WEIGHT = 0.25
EPSILON = 1e-06


def split3(x):
    first = lax.reduce_precision(x, exponent_bits=8, mantissa_bits=7)
    rest = x - first
    second = lax.reduce_precision(rest, exponent_bits=8, mantissa_bits=7)
    third = rest - second
    return first.astype(jnp.bfloat16), second.astype(jnp.bfloat16), third.astype(jnp.bfloat16)


def step_body(embeddings, centroids, rotation):
    high = lax.Precision.HIGH
    width = rotation.shape[0]
    dp_idx = lax.axis_index("dp")

    rot_pieces = jnp.concatenate(split3(rotation), axis=0)
    emb_stacked = jnp.concatenate([embeddings] * 3, axis=1)
    rotated = jnp.dot(emb_stacked, rot_pieces, preferred_element_type=jnp.float32).astype(jnp.bfloat16)

    half_norm = 0.5 * jnp.sum(jnp.square(centroids.astype(jnp.float32)), axis=1)
    score_scale = SHARPNESS / math.sqrt(width)
    raw_scores = lax.dot_general(
        rotated, centroids, (((1,), (1,)), ((), ())), preferred_element_type=jnp.float32
    )
    scores = (raw_scores - half_norm[None, :]) * score_scale
    local_top = jnp.max(scores, axis=1)
    local_total = jnp.sum(jnp.exp(scores - local_top[:, None]), axis=1)
    stats = ring_gather(jnp.stack([local_top, local_total])[None], CENT_GROUPS)
    row_top = jnp.max(stats[:, 0, :], axis=0)
    row_total = jnp.sum(stats[:, 1, :] * jnp.exp(stats[:, 0, :] - row_top[None, :]), axis=0)
    exp_scores = jnp.exp(scores - row_top[:, None])
    weights = (exp_scores / row_total[:, None]).astype(jnp.bfloat16)

    rebuilt = jnp.dot(weights, centroids, preferred_element_type=jnp.float32)
    reb_high = lax.reduce_precision(rebuilt, exponent_bits=8, mantissa_bits=7)
    reb_pieces = jnp.concatenate(
        [reb_high.astype(jnp.bfloat16), (rebuilt - reb_high).astype(jnp.bfloat16)], axis=0
    )
    emb_rows = jnp.concatenate([embeddings] * 2, axis=0)
    partial_value = lax.dot_general(
        emb_rows, reb_pieces, (((0,), (0,)), ((), ())), preferred_element_type=jnp.float32
    )

    cross_gram = ring_psum(partial_value)

    ones = jnp.zeros((rotated.shape[0], 128), jnp.bfloat16).at[:, 0].set(1)
    rotated_ones = jnp.concatenate([rotated, ones], axis=1)
    cent_sums = lax.dot_general(
        weights, rotated_ones, (((0,), (0,)), ((), ())), preferred_element_type=jnp.float32
    )
    share = lax.psum_scatter(cent_sums, "dp", scatter_dimension=0, tiled=True)
    share_sums = share[:, :width]
    share_counts = share[:, width]
    block_rows = share.shape[0]
    first_row = dp_idx * block_rows
    own_centroids = lax.dynamic_slice_in_dim(centroids, first_row, block_rows, 0).astype(
        jnp.float32
    )
    new_centroids = (share_sums + PRIOR_WEIGHT * own_centroids) / (share_counts + PRIOR_WEIGHT)[
        :, None
    ]

    frobenius = jnp.sqrt(jnp.sum(cross_gram * cross_gram) + EPSILON)
    unit_cross = cross_gram / frobenius
    gram_once = jnp.dot(unit_cross.T, unit_cross, precision=high)
    gram_twice = jnp.dot(gram_once, gram_once, precision=high)
    norm_scale = (jnp.sum(gram_twice * gram_twice) + EPSILON) ** 0.125
    iterate = unit_cross / norm_scale
    for iteration in range(NS_ITERS):
        if iteration == 0:
            inner = gram_once / (norm_scale * norm_scale)
        else:
            inner = jnp.dot(iterate.T, iterate, precision=high)
        iterate = 1.5 * iterate - 0.5 * jnp.dot(iterate, inner, precision=high)
    return (new_centroids, iterate)


def solution(mesh):
    in_specs = (P("dp", None), P("cent", None), P())
    out_specs = (P(("cent", "dp"), None), P())
    return jax.shard_map(step_body, mesh=mesh, in_specs=in_specs, out_specs=out_specs, check_vma=False)
```
